32 devices in a mesh: row: 4 (over y, x), col: 8 (over z, core).
Axes of the slice: x: 2, y: 2, z: 4, core: 2. Of those that a mesh axis runs over, the one named last changes fastest.
Arguments:
- frames: bfloat16 [4096, 440], P('col'), may hold values from -6 to 6
- center_picks: int32 [8, 8, 64], P('col'), may hold values from 0 to 511, as said below
- send_counts: int32 [8, 8], P(None, 'col'), may hold values from 0 to 64, as said below
- send_offsets: int32 [8, 8], P(None, 'col'), may hold values from 0 to 256, as said below
Outputs:
- factor_panels: float32 [4, 512, 1024], P('row', 'col')
- trailing: float32 [4, 512, 8, 256], P('row', None, 'col')
The draws below stay inside these ranges and needn't reach their ends.
Inputs may be any that keep to these rules, and one draw needn't show every extreme that they name: `center_picks`: for each owner the entries over all destinations and slots are distinct local frame indices. `send_counts`: for each destination the counts over owners sum to 256; every destination has an owner that fills all 64 slots and one that sends nothing. `send_offsets`: for each destination the owners' segments [offset, offset + count) cover 0 to 255 without intersection, in an order that varies by destination; an owner that sends nothing may start at 256.
All inputs are finite; a program needn't handle non-finite values.
Results may differ from the reference program's by a relative error of at most 0.0003.
Values may be sent and summed in bfloat16 or wider, within the bound.
No kernel may reach another device: no remote copies, remote signals or barrier semaphores. Data moves between devices by JAX's collectives and lax.ppermute only.
A program may use at most 128 MiB of HBM per device.

```python
import jax
import jax.numpy as jnp
from jax import lax

FEAT = 440
PANEL = 256
PANELS = 4
CENT_DEV = 256
CAP = 64
FR_DEV = 512
FRAMES = 4096
CENTERS = 2048
ROWS_DEV = 512
TILES = 8
N_ROW = 4
N_COL = 8


def route_tables(key):
    base_key = jax.random.fold_in(key, 7)
    mean_load = CENT_DEV // N_COL
    half_cap = CAP // 2

    def one_target(target_key):
        order = jax.random.permutation(jax.random.fold_in(target_key, 1), N_COL)
        amount = jax.random.randint(jax.random.fold_in(target_key, 2), (N_COL // 2,), 0, half_cap + 1)
        amount = amount.at[0].set(half_cap)
        delta = jnp.zeros((N_COL,), jnp.int32).at[order[0::2]].add(amount).at[order[1::2]].add(-amount)
        counts_here = (mean_load + delta).astype(jnp.int32)
        scores = jax.random.permutation(jax.random.fold_in(target_key, 3), N_COL).astype(jnp.int32)
        scores = scores.at[order[1]].set(N_COL)
        placing = jnp.argsort(scores, stable=True).astype(jnp.int32)
        ordered = counts_here[placing]
        begins = jnp.cumsum(ordered) - ordered
        offsets_here = jnp.zeros((N_COL,), jnp.int32).at[placing].set(begins.astype(jnp.int32))
        return (counts_here, offsets_here)
    target_keys = jax.random.split(base_key, N_COL)
    counts_all, offsets_all = jax.vmap(one_target)(target_keys)
    return (counts_all.T.astype(jnp.int32), offsets_all.T.astype(jnp.int32))


def draw_send_counts(key, part):
    return route_tables(key)[0]


def draw_send_offsets(key, part):
    return route_tables(key)[1]


def draw_center_picks(key, part):
    owner_keys = jax.random.split(jax.random.fold_in(key, 11), N_COL)
    shuffled = jax.vmap(lambda owner_key: jax.random.permutation(owner_key, FR_DEV))(owner_keys)
    return shuffled.reshape(N_COL, N_COL, CAP).astype(jnp.int32)


def block_scale(stream_key, dims, cuts, smallest, top_value):
    gain, own = 1.0, jax.random.fold_in(stream_key, 6)
    for axis_at, blocks in cuts:
        draws = jnp.exp(jax.random.uniform(jax.random.fold_in(own, axis_at), (blocks,), jnp.float32, smallest / len(cuts), top_value / len(cuts)))
        gain = gain * jnp.repeat(draws, dims[axis_at] // blocks).reshape([-1 if axis == axis_at else 1 for axis in range(len(dims))])
    return gain


def normal_values(stream_key, shape, deviation, bound, shards=(), kind=jnp.bfloat16):
    level = block_scale(stream_key, shape, shards, -0.22, 0.18) if shards else 1.0
    result = jax.random.normal(stream_key, shape, jnp.float32) * deviation * level
    return jnp.minimum(jnp.maximum(result, -bound), bound).astype(kind)


def setup_inputs(seed: int = 0) -> dict:
    seeds = jax.random.split(jax.random.key(seed), 5)
    frames = normal_values(seeds[0], (FRAMES, FEAT), 1.0, 6.0, ((0, 8),))
    center_picks = draw_center_picks(jax.random.fold_in(seeds[4], 71), 0)
    send_counts = draw_send_counts(jax.random.fold_in(seeds[4], 71), 0)
    send_offsets = draw_send_offsets(jax.random.fold_in(seeds[4], 71), 0)
    return {"frames": frames, "center_picks": center_picks, "send_counts": send_counts, "send_offsets": send_offsets}


kernel_scale = 0.6
ridge_shift = 0.1

def gaussian(left_feats, right_feats):
    inner = lax.dot_general(left_feats.astype(jnp.float32), right_feats.astype(jnp.float32), (((1,), (1,)), ((), ())), preferred_element_type=jnp.float32)
    left_norm = jnp.sum(jnp.square(left_feats.astype(jnp.float32)), axis=1)
    right_norm = jnp.sum(jnp.square(right_feats.astype(jnp.float32)), axis=1)
    feat_width = left_feats.shape[1]
    return jnp.exp(-(kernel_scale / feat_width) * (left_norm[:, None] + right_norm[None, :] - 2.0 * inner))

def outer_minus(column, panel_cols, rows_piece):
    return column - lax.dot_general(panel_cols.astype(jnp.float32), rows_piece.astype(jnp.float32), (((1,), (1,)), ((), ())), precision=lax.Precision.HIGHEST, preferred_element_type=jnp.float32)

def make_panel(column, factor, row_tile, panel_step):
    solved = jax.scipy.linalg.solve_triangular(factor, column.T, lower=True).T
    repeated = jnp.tile(factor, (column.shape[0] // factor.shape[0], 1))
    return jnp.where((row_tile > panel_step)[:, None], solved, jnp.where((row_tile == panel_step)[:, None], repeated, jnp.zeros_like(solved)))

def reference(frames, center_picks, send_counts, send_offsets):
    position = jnp.arange(CENT_DEV, dtype=jnp.int32)
    starts = send_offsets.T
    lengths = send_counts.T
    inside = (position[None, :, None] >= starts[:, None, :]) & (position[None, :, None] < (starts + lengths)[:, None, :])
    owners = jnp.arange(N_COL, dtype=jnp.int32)
    source = jnp.sum(jnp.where(inside, owners[None, None, :], 0), axis=2).astype(jnp.int32)
    within = (position[None, :] - jnp.sum(jnp.where(inside, starts[:, None, :], 0), axis=2)).astype(jnp.int32)
    target = owners[:, None]
    local_frame = center_picks[source, target, within]
    feats = frames[(source * FR_DEV + local_frame).astype(jnp.int32)]
    centers = feats.reshape(N_COL, CENT_DEV // PANEL, PANEL, FEAT).transpose(1, 0, 2, 3).reshape(CENTERS, FEAT)
    matrix = gaussian(centers, centers) + ridge_shift * jnp.eye(CENTERS, dtype=jnp.float32)
    row_tile = jnp.arange(CENTERS, dtype=jnp.int32) // PANEL
    panels = []
    for panel_step in range(PANELS):
        column = matrix[:, panel_step * PANEL:(panel_step + 1) * PANEL]
        factor = jnp.linalg.cholesky(column[panel_step * PANEL:(panel_step + 1) * PANEL])
        panel_cols = make_panel(column, factor, row_tile, panel_step)
        panels.append(panel_cols)
        matrix = outer_minus(matrix, panel_cols, panel_cols)
    every_panel = jnp.concatenate(panels, axis=1)
    factor_panels = every_panel.reshape(TILES // N_ROW, N_ROW, PANEL, PANELS * PANEL).transpose(1, 0, 2, 3).reshape(N_ROW, ROWS_DEV, PANELS * PANEL)
    trailing = matrix.reshape(TILES // N_ROW, N_ROW, PANEL, CENT_DEV // PANEL, N_COL, PANEL).transpose(1, 0, 2, 4, 3, 5).reshape(N_ROW, ROWS_DEV, N_COL, CENT_DEV)
    return (factor_panels, trailing)
```

```python
import jax
import jax.numpy as jnp
from jax import lax
from jax.sharding import PartitionSpec as P

PANEL = 256
PANELS = 4
CENT_DEV = 256


kernel_scale = 0.6
ridge_shift = 0.1


def gaussian(left_feats, right_feats):
    inner = lax.dot_general(
        left_feats, right_feats, (((1,), (1,)), ((), ())), preferred_element_type=jnp.float32
    )
    left_norm = jnp.sum(jnp.square(left_feats.astype(jnp.float32)), axis=1)
    right_norm = jnp.sum(jnp.square(right_feats.astype(jnp.float32)), axis=1)
    feat_width = left_feats.shape[1]
    return jnp.exp(
        -(kernel_scale / feat_width) * (left_norm[:, None] + right_norm[None, :] - 2.0 * inner)
    )


def ridged(left_feats, left_index, right_feats, right_index):
    eye = (left_index[:, None] == right_index[None, :]).astype(jnp.float32)
    return gaussian(left_feats, right_feats) + ridge_shift * eye


def matmul_t(left, right):
    return lax.dot_general(
        left,
        right,
        (((1,), (1,)), ((), ())),
        precision=lax.Precision.HIGHEST,
        preferred_element_type=jnp.float32,
    )


def tile_rows(tiles):
    return (tiles[:, None] * PANEL + jnp.arange(PANEL, dtype=jnp.int32)[None, :]).reshape(-1)


def per_device(frames, center_picks, send_counts, send_offsets):
    rows_axis = lax.axis_size("row")
    cols_axis = lax.axis_size("col")
    row_id = lax.axis_index("row")
    col_id = lax.axis_index("col")
    feat_width = frames.shape[1]
    capacity = center_picks.shape[2]
    outgoing = frames[center_picks[0]]
    incoming = lax.all_to_all(outgoing, "col", split_axis=0, concat_axis=0, tiled=True)
    position = jnp.arange(CENT_DEV, dtype=jnp.int32)
    starts = send_offsets[:, 0]
    lengths = send_counts[:, 0]
    inside = (position[:, None] >= starts[None, :]) & (
        position[:, None] < (starts + lengths)[None, :]
    )
    source = jnp.sum(jnp.where(inside, jnp.arange(cols_axis, dtype=jnp.int32)[None, :], 0), axis=1)
    within = position - jnp.sum(jnp.where(inside, starts[None, :], 0), axis=1)
    own_feats = incoming.reshape(cols_axis * capacity, feat_width)[source * capacity + within]
    col_slots = CENT_DEV // PANEL
    row_tiles_dev = col_slots * cols_axis // rows_axis
    gathered = lax.all_gather(own_feats, "col", axis=0, tiled=True)
    centers = (
        gathered.reshape(cols_axis, col_slots, PANEL, feat_width)
        .transpose(1, 0, 2, 3)
        .reshape(cols_axis * col_slots * PANEL, feat_width)
    )
    panel_tiles = jnp.arange(PANELS, dtype=jnp.int32)
    my_row_tiles = row_id + rows_axis * jnp.arange(row_tiles_dev, dtype=jnp.int32)
    my_col_tiles = col_id + cols_axis * jnp.arange(col_slots, dtype=jnp.int32)
    ext_tiles = jnp.concatenate([panel_tiles, my_row_tiles, my_col_tiles])
    ext_index = tile_rows(ext_tiles)
    panel_index = tile_rows(panel_tiles)
    ext_feats = centers[ext_index]
    panel_feats = centers[:PANELS * PANEL]
    kernel = ridged(ext_feats, ext_index, panel_feats, panel_index)
    ext_tile = ext_index // PANEL
    columns = [kernel[:, q * PANEL : (q + 1) * PANEL] for q in range(PANELS)]
    panels = []
    for panel_step in range(PANELS):
        column = columns[panel_step]
        diag_block = column[panel_step * PANEL : (panel_step + 1) * PANEL]
        factor = jnp.linalg.cholesky(diag_block)
        solved = lax.linalg.triangular_solve(
            factor, column, left_side=False, lower=True, transpose_a=True
        )
        repeated = jnp.tile(factor, (column.shape[0] // PANEL, 1))
        panel = jnp.where(
            (ext_tile > panel_step)[:, None],
            solved,
            jnp.where((ext_tile == panel_step)[:, None], repeated, jnp.zeros_like(solved)),
        )
        panels.append(panel)
        for later in range(panel_step + 1, PANELS):
            columns[later] = columns[later] - matmul_t(
                panel, panel[later * PANEL : (later + 1) * PANEL]
            )
    every_panel = jnp.concatenate(panels, axis=1)
    base = PANELS * PANEL
    rows_dev = row_tiles_dev * PANEL
    row_panel = every_panel[base : base + rows_dev]
    col_panel = every_panel[base + rows_dev :]
    row_index = ext_index[base : base + rows_dev]
    col_index = ext_index[base + rows_dev :]
    block = ridged(ext_feats[base : base + rows_dev], row_index, ext_feats[base + rows_dev :], col_index)
    trailing = (block - matmul_t(row_panel, col_panel)).reshape(1, rows_dev, 1, CENT_DEV)
    share_rows = rows_dev // cols_axis
    panel_share = lax.dynamic_slice_in_dim(row_panel, col_id * share_rows, share_rows, 0).reshape(
        1, share_rows, PANELS * PANEL
    )
    return (panel_share, trailing)


def solution(mesh):
    in_specs = (P("col", None), P("col", None, None), P(None, "col"), P(None, "col"))
    out_specs = (P("row", "col", None), P("row", None, "col", None))
    return jax.shard_map(
        per_device, mesh=mesh, in_specs=in_specs, out_specs=out_specs, check_vma=False
    )
```

```python
import jax
import jax.numpy as jnp
from jax import lax
from jax.experimental import pallas as pl
from jax.experimental.pallas import tpu as pltpu
from jax.sharding import PartitionSpec as P

PANEL = 256
PANELS = 4
BLOCK = 128
CENT_DEV = 256


kernel_scale = 0.6
ridge_shift = 0.1


def gaussian(left_feats, right_feats):
    inner = lax.dot_general(
        left_feats, right_feats, (((1,), (1,)), ((), ())), preferred_element_type=jnp.float32
    )
    left_norm = jnp.sum(jnp.square(left_feats.astype(jnp.float32)), axis=1)
    right_norm = jnp.sum(jnp.square(right_feats.astype(jnp.float32)), axis=1)
    feat_width = left_feats.shape[1]
    return jnp.exp(
        -(kernel_scale / feat_width) * (left_norm[:, None] + right_norm[None, :] - 2.0 * inner)
    )


def ridged(left_feats, left_index, right_feats, right_index):
    eye = (left_index[:, None] == right_index[None, :]).astype(jnp.float32)
    return gaussian(left_feats, right_feats) + ridge_shift * eye


def matmul_t(left, right):
    return lax.dot_general(
        left,
        right,
        (((1,), (1,)), ((), ())),
        precision=lax.Precision.HIGHEST,
        preferred_element_type=jnp.float32,
    )


def _chol_inv_kernel(a_ref, lt_ref, linv_ref, w_ref):
    n = a_ref.shape[0]
    a = a_ref[...]
    row_i = lax.broadcasted_iota(jnp.int32, (n, n), 0)
    col_i = lax.broadcasted_iota(jnp.int32, (n, n), 1)
    w_ref[:, :n] = a
    w_ref[:, n:] = jnp.where(row_i == col_i, 1.0, 0.0).astype(jnp.float32)
    lane_row = lax.broadcasted_iota(jnp.int32, (1, 2 * n), 1)
    sub_w = lax.broadcasted_iota(jnp.int32, (n, 2 * n), 0)
    sub_col = lax.broadcasted_iota(jnp.int32, (n, 1), 0)

    def body(j, carry):
        w = w_ref[...]
        rowj = w_ref[pl.ds(j, 1), :]
        piv = jnp.sum(jnp.where(lane_row == j, rowj, 0.0), axis=1, keepdims=True)
        r = 1.0 / jnp.sqrt(piv)
        srow = rowj * r
        colj = jnp.sum(jnp.where(col_i == j, w[:, :n], 0.0), axis=1, keepdims=True)
        m = jnp.where(sub_col > j, colj * r, 0.0)
        neww = jnp.where(sub_w == j, srow, w - m * srow)
        w_ref[...] = neww
        return carry

    lax.fori_loop(0, n, body, 0)
    w = w_ref[...]
    lt_ref[...] = jnp.where(col_i >= row_i, w[:, :n], 0.0)
    linv_ref[...] = jnp.where(col_i <= row_i, w[:, n:], 0.0)


def chol_inv(a):
    n = a.shape[0]
    return pl.pallas_call(
        _chol_inv_kernel,
        out_shape=(jax.ShapeDtypeStruct((n, n), jnp.float32), jax.ShapeDtypeStruct((n, n), jnp.float32)),
        scratch_shapes=[pltpu.VMEM((n, 2 * n), jnp.float32)],
    )(a)


def tile_rows(tiles):
    return (tiles[:, None] * PANEL + jnp.arange(PANEL, dtype=jnp.int32)[None, :]).reshape(-1)


def per_device(frames, center_picks, send_counts, send_offsets):
    rows_axis = lax.axis_size("row")
    cols_axis = lax.axis_size("col")
    row_id = lax.axis_index("row")
    col_id = lax.axis_index("col")
    feat_width = frames.shape[1]
    capacity = center_picks.shape[2]
    outgoing = frames[center_picks[0]]
    incoming = lax.all_to_all(outgoing, "col", split_axis=0, concat_axis=0, tiled=True)
    position = jnp.arange(CENT_DEV, dtype=jnp.int32)
    starts = send_offsets[:, 0]
    lengths = send_counts[:, 0]
    inside = (position[:, None] >= starts[None, :]) & (
        position[:, None] < (starts + lengths)[None, :]
    )
    source = jnp.sum(jnp.where(inside, jnp.arange(cols_axis, dtype=jnp.int32)[None, :], 0), axis=1)
    within = position - jnp.sum(jnp.where(inside, starts[None, :], 0), axis=1)
    own_feats = incoming.reshape(cols_axis * capacity, feat_width)[source * capacity + within]
    col_slots = CENT_DEV // PANEL
    row_tiles_dev = col_slots * cols_axis // rows_axis
    gathered = lax.all_gather(own_feats, "col", axis=0, tiled=True)
    centers = (
        gathered.reshape(cols_axis, col_slots, PANEL, feat_width)
        .transpose(1, 0, 2, 3)
        .reshape(cols_axis * col_slots * PANEL, feat_width)
    )
    panel_tiles = jnp.arange(PANELS, dtype=jnp.int32)
    my_row_tiles = row_id + rows_axis * jnp.arange(row_tiles_dev, dtype=jnp.int32)
    my_col_tiles = col_id + cols_axis * jnp.arange(col_slots, dtype=jnp.int32)
    ext_tiles = jnp.concatenate([panel_tiles, my_row_tiles, my_col_tiles])
    ext_index = tile_rows(ext_tiles)
    panel_index = tile_rows(panel_tiles)
    ext_feats = jnp.concatenate(
        [centers[: PANELS * PANEL]]
        + [
            lax.dynamic_slice_in_dim(centers, tile * PANEL, PANEL, 0)
            for tile in list(my_row_tiles) + list(my_col_tiles)
        ],
        axis=0,
    )
    panel_feats = centers[: PANELS * PANEL]
    kernel = ridged(ext_feats, ext_index, panel_feats, panel_index)
    ext_block = ext_index // BLOCK
    rest = kernel
    panels = []
    for step in range(PANELS * PANEL // BLOCK):
        column = rest[:, :BLOCK]
        diag_block = column[step * BLOCK : (step + 1) * BLOCK]
        diag_block = (diag_block + diag_block.T) * 0.5
        upper, inverse = chol_inv(diag_block)
        factor = upper.T
        solved = matmul_t(column, inverse)
        repeated = jnp.tile(factor, (column.shape[0] // BLOCK, 1))
        panel = jnp.where(
            (ext_block > step)[:, None],
            solved,
            jnp.where((ext_block == step)[:, None], repeated, jnp.zeros_like(solved)),
        )
        panels.append(panel)
        if rest.shape[1] > BLOCK:
            rest = rest[:, BLOCK:] - matmul_t(panel, panel[(step + 1) * BLOCK : PANELS * PANEL])
    every_panel = jnp.concatenate(panels, axis=1)
    base = PANELS * PANEL
    rows_dev = row_tiles_dev * PANEL
    row_panel = every_panel[base : base + rows_dev]
    col_panel = every_panel[base + rows_dev :]
    row_index = ext_index[base : base + rows_dev]
    col_index = ext_index[base + rows_dev :]
    block = ridged(ext_feats[base : base + rows_dev], row_index, ext_feats[base + rows_dev :], col_index)
    trailing = (block - matmul_t(row_panel, col_panel)).reshape(1, rows_dev, 1, CENT_DEV)
    share_rows = rows_dev // cols_axis
    panel_share = lax.dynamic_slice_in_dim(row_panel, col_id * share_rows, share_rows, 0).reshape(
        1, share_rows, PANELS * PANEL
    )
    return (panel_share, trailing)


def solution(mesh):
    in_specs = (P("col", None), P("col", None, None), P(None, "col"), P(None, "col"))
    out_specs = (P("row", "col", None), P("row", None, "col", None))
    return jax.shard_map(
        per_device, mesh=mesh, in_specs=in_specs, out_specs=out_specs, check_vma=False
    )
```

```python
import jax
import jax.numpy as jnp
from jax import lax
from jax.experimental import pallas as pl
from jax.experimental.pallas import tpu as pltpu
from jax.sharding import PartitionSpec as P

PANEL = 256
PANELS = 4
BLOCK = 128
CHUNK = 256
CENT_DEV = 256


kernel_scale = 0.6
ridge_shift = 0.1


def gaussian(left_feats, right_feats):
    inner = lax.dot_general(
        left_feats, right_feats, (((1,), (1,)), ((), ())), preferred_element_type=jnp.float32
    )
    left_norm = jnp.sum(jnp.square(left_feats.astype(jnp.float32)), axis=1)
    right_norm = jnp.sum(jnp.square(right_feats.astype(jnp.float32)), axis=1)
    feat_width = left_feats.shape[1]
    return jnp.exp(
        -(kernel_scale / feat_width) * (left_norm[:, None] + right_norm[None, :] - 2.0 * inner)
    )


def ridged(left_feats, left_index, right_feats, right_index):
    eye = (left_index[:, None] == right_index[None, :]).astype(jnp.float32)
    return gaussian(left_feats, right_feats) + ridge_shift * eye


def matmul_t(left, right):
    return lax.dot_general(
        left,
        right,
        (((1,), (1,)), ((), ())),
        precision=lax.Precision.HIGHEST,
        preferred_element_type=jnp.float32,
    )


def _dot_t(left, right):
    return lax.dot_general(
        left, right, (((1,), (1,)), ((), ())),
        precision=lax.Precision.HIGHEST, preferred_element_type=jnp.float32,
    )


def _factor_kernel(m_ref, blk_ref, p_ref, w_ref):
    rows, width = m_ref.shape
    n = BLOCK
    row_i = lax.broadcasted_iota(jnp.int32, (n, n), 0)
    col_i = lax.broadcasted_iota(jnp.int32, (n, n), 1)
    eye = jnp.where(row_i == col_i, 1.0, 0.0).astype(jnp.float32)
    lane_row = lax.broadcasted_iota(jnp.int32, (1, 2 * n), 1)
    sub_w = lax.broadcasted_iota(jnp.int32, (n, 2 * n), 0)
    sub_col = lax.broadcasted_iota(jnp.int32, (n, 1), 0)

    def body(j, carry):
        w = w_ref[...]
        rowj = w_ref[pl.ds(j, 1), :]
        piv = jnp.sum(jnp.where(lane_row == j, rowj, 0.0), axis=1, keepdims=True)
        r = 1.0 / jnp.sqrt(piv)
        srow = rowj * r
        colj = jnp.sum(jnp.where(col_i == j, w[:, :n], 0.0), axis=1, keepdims=True)
        m = jnp.where(sub_col > j, colj * r, 0.0)
        w_ref[...] = jnp.where(sub_w == j, srow, w - m * srow)
        return carry

    for step in range(width // n):
        c0 = step * n
        diag = m_ref[c0 : c0 + n, c0 : c0 + n]
        w_ref[:, :n] = (diag + diag.T) * 0.5
        w_ref[:, n:] = eye
        lax.fori_loop(0, n, body, 0)
        w = w_ref[...]
        factor = jnp.where(col_i >= row_i, w[:, :n], 0.0).T
        inverse = jnp.where(col_i <= row_i, w[:, n:], 0.0)
        for r0 in range(0, rows, CHUNK):
            column = m_ref[r0 : r0 + CHUNK, c0 : c0 + n]
            solved = _dot_t(column, inverse)
            blk = blk_ref[r0 : r0 + CHUNK, :]
            tiled = jnp.concatenate([factor] * (CHUNK // n), axis=0)
            p_ref[r0 : r0 + CHUNK, c0 : c0 + n] = jnp.where(
                blk > step, solved, jnp.where(blk == step, tiled, 0.0)
            )
        if c0 + n < width:
            later = p_ref[c0 + n : width, c0 : c0 + n]
            for r0 in range(0, rows, CHUNK):
                m_ref[r0 : r0 + CHUNK, c0 + n : width] = m_ref[r0 : r0 + CHUNK, c0 + n : width] - _dot_t(
                    p_ref[r0 : r0 + CHUNK, c0 : c0 + n], later
                )


def factor_rows(kernel_rows, row_block):
    rows, width = kernel_rows.shape
    return pl.pallas_call(
        _factor_kernel,
        out_shape=jax.ShapeDtypeStruct((rows, width), jnp.float32),
        scratch_shapes=[pltpu.VMEM((BLOCK, 2 * BLOCK), jnp.float32)],
        input_output_aliases={},
    )(kernel_rows, row_block)


def tile_rows(tiles):
    return (tiles[:, None] * PANEL + jnp.arange(PANEL, dtype=jnp.int32)[None, :]).reshape(-1)


def per_device(frames, center_picks, send_counts, send_offsets):
    rows_axis = lax.axis_size("row")
    cols_axis = lax.axis_size("col")
    row_id = lax.axis_index("row")
    col_id = lax.axis_index("col")
    feat_width = frames.shape[1]
    capacity = center_picks.shape[2]
    outgoing = frames[center_picks[0]]
    incoming = lax.all_to_all(outgoing, "col", split_axis=0, concat_axis=0, tiled=True)
    position = jnp.arange(CENT_DEV, dtype=jnp.int32)
    starts = send_offsets[:, 0]
    lengths = send_counts[:, 0]
    inside = (position[:, None] >= starts[None, :]) & (
        position[:, None] < (starts + lengths)[None, :]
    )
    source = jnp.sum(jnp.where(inside, jnp.arange(cols_axis, dtype=jnp.int32)[None, :], 0), axis=1)
    within = position - jnp.sum(jnp.where(inside, starts[None, :], 0), axis=1)
    own_feats = incoming.reshape(cols_axis * capacity, feat_width)[source * capacity + within]
    col_slots = CENT_DEV // PANEL
    row_tiles_dev = col_slots * cols_axis // rows_axis
    gathered = lax.all_gather(own_feats, "col", axis=0, tiled=True)
    centers = (
        gathered.reshape(cols_axis, col_slots, PANEL, feat_width)
        .transpose(1, 0, 2, 3)
        .reshape(cols_axis * col_slots * PANEL, feat_width)
    )
    panel_tiles = jnp.arange(PANELS, dtype=jnp.int32)
    my_row_tiles = row_id + rows_axis * jnp.arange(row_tiles_dev, dtype=jnp.int32)
    my_col_tiles = col_id + cols_axis * jnp.arange(col_slots, dtype=jnp.int32)
    ext_tiles = jnp.concatenate([panel_tiles, my_row_tiles, my_col_tiles])
    ext_index = tile_rows(ext_tiles)
    panel_index = tile_rows(panel_tiles)
    ext_feats = jnp.concatenate(
        [centers[: PANELS * PANEL]]
        + [
            lax.dynamic_slice_in_dim(centers, tile * PANEL, PANEL, 0)
            for tile in list(my_row_tiles) + list(my_col_tiles)
        ],
        axis=0,
    )
    panel_feats = centers[: PANELS * PANEL]
    kernel = ridged(ext_feats, ext_index, panel_feats, panel_index)
    every_panel = factor_rows(kernel, (ext_index // BLOCK)[:, None])
    base = PANELS * PANEL
    rows_dev = row_tiles_dev * PANEL
    row_panel = every_panel[base : base + rows_dev]
    col_panel = every_panel[base + rows_dev :]
    row_index = ext_index[base : base + rows_dev]
    col_index = ext_index[base + rows_dev :]
    block = ridged(ext_feats[base : base + rows_dev], row_index, ext_feats[base + rows_dev :], col_index)
    trailing = (block - matmul_t(row_panel, col_panel)).reshape(1, rows_dev, 1, CENT_DEV)
    share_rows = rows_dev // cols_axis
    panel_share = lax.dynamic_slice_in_dim(row_panel, col_id * share_rows, share_rows, 0).reshape(
        1, share_rows, PANELS * PANEL
    )
    return (panel_share, trailing)


def solution(mesh):
    in_specs = (P("col", None), P("col", None, None), P(None, "col"), P(None, "col"))
    out_specs = (P("row", "col", None), P("row", None, "col", None))
    return jax.shard_map(
        per_device, mesh=mesh, in_specs=in_specs, out_specs=out_specs, check_vma=False
    )
```

```python
import jax
import jax.numpy as jnp
from jax import lax
from jax.experimental import pallas as pl
from jax.experimental.pallas import tpu as pltpu
from jax.sharding import PartitionSpec as P

PANEL = 256
PANELS = 4
BLOCK = 128
CHUNK = 256
UNROLL = 8
CENT_DEV = 256


kernel_scale = 0.6
ridge_shift = 0.1


def gaussian(left_feats, right_feats):
    inner = lax.dot_general(
        left_feats, right_feats, (((1,), (1,)), ((), ())), preferred_element_type=jnp.float32
    )
    left_norm = jnp.sum(jnp.square(left_feats.astype(jnp.float32)), axis=1)
    right_norm = jnp.sum(jnp.square(right_feats.astype(jnp.float32)), axis=1)
    feat_width = left_feats.shape[1]
    return jnp.exp(
        -(kernel_scale / feat_width) * (left_norm[:, None] + right_norm[None, :] - 2.0 * inner)
    )


def ridged(left_feats, left_index, right_feats, right_index):
    eye = (left_index[:, None] == right_index[None, :]).astype(jnp.float32)
    return gaussian(left_feats, right_feats) + ridge_shift * eye


def matmul_t(left, right):
    return lax.dot_general(
        left,
        right,
        (((1,), (1,)), ((), ())),
        precision=lax.Precision.HIGHEST,
        preferred_element_type=jnp.float32,
    )


def _dot_t(left, right):
    return lax.dot_general(
        left, right, (((1,), (1,)), ((), ())),
        precision=lax.Precision.HIGHEST, preferred_element_type=jnp.float32,
    )


def _factor_kernel(m_ref, blk_ref, p_ref, w_ref):
    rows, width = m_ref.shape
    n = BLOCK
    row_i = lax.broadcasted_iota(jnp.int32, (n, n), 0)
    col_i = lax.broadcasted_iota(jnp.int32, (n, n), 1)
    eye = jnp.where(row_i == col_i, 1.0, 0.0).astype(jnp.float32)
    lane_row = lax.broadcasted_iota(jnp.int32, (1, 2 * n), 1)
    sub_w = lax.broadcasted_iota(jnp.int32, (n, 2 * n), 0)
    sub_col = lax.broadcasted_iota(jnp.int32, (n, 1), 0)

    def body(j, piv):
        w = w_ref[...]
        rowj = w_ref[pl.ds(j, 1), :]
        jn = jnp.minimum(j + 1, n - 1)
        rown = w_ref[pl.ds(jn, 1), :]
        r = 1.0 / jnp.sqrt(piv)
        srow = rowj * r
        colj = jnp.sum(jnp.where(col_i == j, w[:, :n], 0.0), axis=1, keepdims=True)
        m = jnp.where(sub_col > j, colj * r, 0.0)
        w_ref[...] = jnp.where(sub_w == j, srow, w - m * srow)
        a = jnp.sum(jnp.where(lane_row == jn, rown, 0.0), axis=1, keepdims=True)
        b = jnp.sum(jnp.where(lane_row == jn, rowj, 0.0), axis=1, keepdims=True) * r
        return a - b * b

    for step in range(width // n):
        c0 = step * n
        diag = m_ref[c0 : c0 + n, c0 : c0 + n]
        diag = (diag + diag.T) * 0.5
        w_ref[:, :n] = diag
        w_ref[:, n:] = eye
        piv0 = jnp.sum(jnp.where(row_i[0:1] == col_i[0:1], diag[0:1], 0.0), axis=1, keepdims=True)
        lax.fori_loop(0, n, body, piv0, unroll=UNROLL)
        w = w_ref[...]
        factor = jnp.where(col_i >= row_i, w[:, :n], 0.0).T
        inverse = jnp.where(col_i <= row_i, w[:, n:], 0.0)
        for r0 in range(0, rows, CHUNK):
            column = m_ref[r0 : r0 + CHUNK, c0 : c0 + n]
            solved = _dot_t(column, inverse)
            blk = blk_ref[r0 : r0 + CHUNK, :]
            tiled = jnp.concatenate([factor] * (CHUNK // n), axis=0)
            p_ref[r0 : r0 + CHUNK, c0 : c0 + n] = jnp.where(
                blk > step, solved, jnp.where(blk == step, tiled, 0.0)
            )
        if c0 + n < width:
            later = p_ref[c0 + n : width, c0 : c0 + n]
            for r0 in range(0, rows, CHUNK):
                m_ref[r0 : r0 + CHUNK, c0 + n : width] = m_ref[r0 : r0 + CHUNK, c0 + n : width] - _dot_t(
                    p_ref[r0 : r0 + CHUNK, c0 : c0 + n], later
                )


def factor_rows(kernel_rows, row_block):
    rows, width = kernel_rows.shape
    return pl.pallas_call(
        _factor_kernel,
        out_shape=jax.ShapeDtypeStruct((rows, width), jnp.float32),
        scratch_shapes=[pltpu.VMEM((BLOCK, 2 * BLOCK), jnp.float32)],
        input_output_aliases={},
    )(kernel_rows, row_block)


def tile_rows(tiles):
    return (tiles[:, None] * PANEL + jnp.arange(PANEL, dtype=jnp.int32)[None, :]).reshape(-1)


def per_device(frames, center_picks, send_counts, send_offsets):
    rows_axis = lax.axis_size("row")
    cols_axis = lax.axis_size("col")
    row_id = lax.axis_index("row")
    col_id = lax.axis_index("col")
    feat_width = frames.shape[1]
    capacity = center_picks.shape[2]
    outgoing = frames[center_picks[0]]
    incoming = lax.all_to_all(outgoing, "col", split_axis=0, concat_axis=0, tiled=True)
    position = jnp.arange(CENT_DEV, dtype=jnp.int32)
    starts = send_offsets[:, 0]
    lengths = send_counts[:, 0]
    inside = (position[:, None] >= starts[None, :]) & (
        position[:, None] < (starts + lengths)[None, :]
    )
    source = jnp.sum(jnp.where(inside, jnp.arange(cols_axis, dtype=jnp.int32)[None, :], 0), axis=1)
    within = position - jnp.sum(jnp.where(inside, starts[None, :], 0), axis=1)
    own_feats = incoming.reshape(cols_axis * capacity, feat_width)[source * capacity + within]
    col_slots = CENT_DEV // PANEL
    row_tiles_dev = col_slots * cols_axis // rows_axis
    gathered = lax.all_gather(own_feats, "col", axis=0, tiled=True)
    centers = (
        gathered.reshape(cols_axis, col_slots, PANEL, feat_width)
        .transpose(1, 0, 2, 3)
        .reshape(cols_axis * col_slots * PANEL, feat_width)
    )
    panel_tiles = jnp.arange(PANELS, dtype=jnp.int32)
    my_row_tiles = row_id + rows_axis * jnp.arange(row_tiles_dev, dtype=jnp.int32)
    my_col_tiles = col_id + cols_axis * jnp.arange(col_slots, dtype=jnp.int32)
    ext_tiles = jnp.concatenate([panel_tiles, my_row_tiles, my_col_tiles])
    ext_index = tile_rows(ext_tiles)
    panel_index = tile_rows(panel_tiles)
    ext_feats = jnp.concatenate(
        [centers[: PANELS * PANEL]]
        + [
            lax.dynamic_slice_in_dim(centers, tile * PANEL, PANEL, 0)
            for tile in list(my_row_tiles) + list(my_col_tiles)
        ],
        axis=0,
    )
    panel_feats = centers[: PANELS * PANEL]
    kernel = ridged(ext_feats, ext_index, panel_feats, panel_index)
    every_panel = factor_rows(kernel, (ext_index // BLOCK)[:, None])
    base = PANELS * PANEL
    rows_dev = row_tiles_dev * PANEL
    row_panel = every_panel[base : base + rows_dev]
    col_panel = every_panel[base + rows_dev :]
    row_index = ext_index[base : base + rows_dev]
    col_index = ext_index[base + rows_dev :]
    block = ridged(ext_feats[base : base + rows_dev], row_index, ext_feats[base + rows_dev :], col_index)
    trailing = (block - matmul_t(row_panel, col_panel)).reshape(1, rows_dev, 1, CENT_DEV)
    share_rows = rows_dev // cols_axis
    panel_share = lax.dynamic_slice_in_dim(row_panel, col_id * share_rows, share_rows, 0).reshape(
        1, share_rows, PANELS * PANEL
    )
    return (panel_share, trailing)


def solution(mesh):
    in_specs = (P("col", None), P("col", None, None), P(None, "col"), P(None, "col"))
    out_specs = (P("row", "col", None), P("row", None, "col", None))
    return jax.shard_map(
        per_device, mesh=mesh, in_specs=in_specs, out_specs=out_specs, check_vma=False
    )
```

```python
import jax
import jax.numpy as jnp
from jax import lax
from jax.experimental import pallas as pl
from jax.experimental.pallas import tpu as pltpu
from jax.sharding import PartitionSpec as P

PANEL = 256
PANELS = 4
BLOCK = 128
CHUNK = 256
SEG = 8
CENT_DEV = 256


kernel_scale = 0.6
ridge_shift = 0.1


def gaussian(left_feats, right_feats):
    inner = lax.dot_general(
        left_feats, right_feats, (((1,), (1,)), ((), ())), preferred_element_type=jnp.float32
    )
    left_norm = jnp.sum(jnp.square(left_feats.astype(jnp.float32)), axis=1)
    right_norm = jnp.sum(jnp.square(right_feats.astype(jnp.float32)), axis=1)
    feat_width = left_feats.shape[1]
    return jnp.exp(
        -(kernel_scale / feat_width) * (left_norm[:, None] + right_norm[None, :] - 2.0 * inner)
    )


def ridged(left_feats, left_index, right_feats, right_index):
    eye = (left_index[:, None] == right_index[None, :]).astype(jnp.float32)
    return gaussian(left_feats, right_feats) + ridge_shift * eye


def matmul_t(left, right):
    return lax.dot_general(
        left,
        right,
        (((1,), (1,)), ((), ())),
        precision=lax.Precision.HIGHEST,
        preferred_element_type=jnp.float32,
    )


def _dot_t(left, right):
    return lax.dot_general(
        left, right, (((1,), (1,)), ((), ())),
        precision=lax.Precision.HIGHEST, preferred_element_type=jnp.float32,
    )


def _factor_kernel(m_ref, blk_ref, p_ref, w_ref):
    rows, width = m_ref.shape
    n = BLOCK
    row_i = lax.broadcasted_iota(jnp.int32, (n, n), 0)
    col_i = lax.broadcasted_iota(jnp.int32, (n, n), 1)
    eye = jnp.where(row_i == col_i, 1.0, 0.0).astype(jnp.float32)
    lane_row = lax.broadcasted_iota(jnp.int32, (1, 2 * n), 1)

    def segment(start, piv):
        high = n - start
        sub_w = lax.broadcasted_iota(jnp.int32, (high, 2 * n), 0) + start
        sub_col = lax.broadcasted_iota(jnp.int32, (high, 1), 0) + start
        col_s = lax.broadcasted_iota(jnp.int32, (high, n), 1)

        def body(j, piv):
            w = w_ref[start:, :]
            rowj = w_ref[pl.ds(j, 1), :]
            jn = jnp.minimum(j + 1, n - 1)
            rown = w_ref[pl.ds(jn, 1), :]
            r = 1.0 / jnp.sqrt(piv)
            srow = rowj * r
            colj = jnp.sum(jnp.where(col_s == j, w[:, :n], 0.0), axis=1, keepdims=True)
            m = jnp.where(sub_col > j, colj * r, 0.0)
            w_ref[start:, :] = jnp.where(sub_w == j, srow, w - m * srow)
            a = jnp.sum(jnp.where(lane_row == jn, rown, 0.0), axis=1, keepdims=True)
            b = jnp.sum(jnp.where(lane_row == jn, rowj, 0.0), axis=1, keepdims=True) * r
            return a - b * b

        return lax.fori_loop(start, start + SEG, body, piv, unroll=SEG)

    for step in range(width // n):
        c0 = step * n
        diag = m_ref[c0 : c0 + n, c0 : c0 + n]
        diag = (diag + diag.T) * 0.5
        w_ref[:, :n] = diag
        w_ref[:, n:] = eye
        piv0 = jnp.sum(jnp.where(row_i[0:1] == col_i[0:1], diag[0:1], 0.0), axis=1, keepdims=True)
        piv = piv0
        for start in range(0, n, SEG):
            piv = segment(start, piv)
        w = w_ref[...]
        factor = jnp.where(col_i >= row_i, w[:, :n], 0.0).T
        inverse = jnp.where(col_i <= row_i, w[:, n:], 0.0)
        for r0 in range(0, rows, CHUNK):
            column = m_ref[r0 : r0 + CHUNK, c0 : c0 + n]
            solved = _dot_t(column, inverse)
            blk = blk_ref[r0 : r0 + CHUNK, :]
            tiled = jnp.concatenate([factor] * (CHUNK // n), axis=0)
            p_ref[r0 : r0 + CHUNK, c0 : c0 + n] = jnp.where(
                blk > step, solved, jnp.where(blk == step, tiled, 0.0)
            )
        if c0 + n < width:
            later = p_ref[c0 + n : width, c0 : c0 + n]
            for r0 in range(0, rows, CHUNK):
                m_ref[r0 : r0 + CHUNK, c0 + n : width] = m_ref[r0 : r0 + CHUNK, c0 + n : width] - _dot_t(
                    p_ref[r0 : r0 + CHUNK, c0 : c0 + n], later
                )


def factor_rows(kernel_rows, row_block):
    rows, width = kernel_rows.shape
    return pl.pallas_call(
        _factor_kernel,
        out_shape=jax.ShapeDtypeStruct((rows, width), jnp.float32),
        scratch_shapes=[pltpu.VMEM((BLOCK, 2 * BLOCK), jnp.float32)],
        input_output_aliases={},
    )(kernel_rows, row_block)


def tile_rows(tiles):
    return (tiles[:, None] * PANEL + jnp.arange(PANEL, dtype=jnp.int32)[None, :]).reshape(-1)


def per_device(frames, center_picks, send_counts, send_offsets):
    rows_axis = lax.axis_size("row")
    cols_axis = lax.axis_size("col")
    row_id = lax.axis_index("row")
    col_id = lax.axis_index("col")
    feat_width = frames.shape[1]
    capacity = center_picks.shape[2]
    outgoing = frames[center_picks[0]]
    incoming = lax.all_to_all(outgoing, "col", split_axis=0, concat_axis=0, tiled=True)
    position = jnp.arange(CENT_DEV, dtype=jnp.int32)
    starts = send_offsets[:, 0]
    lengths = send_counts[:, 0]
    inside = (position[:, None] >= starts[None, :]) & (
        position[:, None] < (starts + lengths)[None, :]
    )
    source = jnp.sum(jnp.where(inside, jnp.arange(cols_axis, dtype=jnp.int32)[None, :], 0), axis=1)
    within = position - jnp.sum(jnp.where(inside, starts[None, :], 0), axis=1)
    own_feats = incoming.reshape(cols_axis * capacity, feat_width)[source * capacity + within]
    col_slots = CENT_DEV // PANEL
    row_tiles_dev = col_slots * cols_axis // rows_axis
    gathered = lax.all_gather(own_feats, "col", axis=0, tiled=True)
    centers = (
        gathered.reshape(cols_axis, col_slots, PANEL, feat_width)
        .transpose(1, 0, 2, 3)
        .reshape(cols_axis * col_slots * PANEL, feat_width)
    )
    panel_tiles = jnp.arange(PANELS, dtype=jnp.int32)
    my_row_tiles = row_id + rows_axis * jnp.arange(row_tiles_dev, dtype=jnp.int32)
    my_col_tiles = col_id + cols_axis * jnp.arange(col_slots, dtype=jnp.int32)
    ext_tiles = jnp.concatenate([panel_tiles, my_row_tiles, my_col_tiles])
    ext_index = tile_rows(ext_tiles)
    panel_index = tile_rows(panel_tiles)
    ext_feats = jnp.concatenate(
        [centers[: PANELS * PANEL]]
        + [
            lax.dynamic_slice_in_dim(centers, tile * PANEL, PANEL, 0)
            for tile in list(my_row_tiles) + list(my_col_tiles)
        ],
        axis=0,
    )
    panel_feats = centers[: PANELS * PANEL]
    kernel = ridged(ext_feats, ext_index, panel_feats, panel_index)
    every_panel = factor_rows(kernel, (ext_index // BLOCK)[:, None])
    base = PANELS * PANEL
    rows_dev = row_tiles_dev * PANEL
    row_panel = every_panel[base : base + rows_dev]
    col_panel = every_panel[base + rows_dev :]
    row_index = ext_index[base : base + rows_dev]
    col_index = ext_index[base + rows_dev :]
    block = ridged(ext_feats[base : base + rows_dev], row_index, ext_feats[base + rows_dev :], col_index)
    trailing = (block - matmul_t(row_panel, col_panel)).reshape(1, rows_dev, 1, CENT_DEV)
    share_rows = rows_dev // cols_axis
    panel_share = lax.dynamic_slice_in_dim(row_panel, col_id * share_rows, share_rows, 0).reshape(
        1, share_rows, PANELS * PANEL
    )
    return (panel_share, trailing)


def solution(mesh):
    in_specs = (P("col", None), P("col", None, None), P(None, "col"), P(None, "col"))
    out_specs = (P("row", "col", None), P("row", None, "col", None))
    return jax.shard_map(
        per_device, mesh=mesh, in_specs=in_specs, out_specs=out_specs, check_vma=False
    )
```

```python
import jax
import jax.numpy as jnp
from jax import lax
from jax.experimental import pallas as pl
from jax.experimental.pallas import tpu as pltpu
from jax.sharding import PartitionSpec as P

PANEL = 256
PANELS = 4
BLOCK = 128
CHUNK = 256
SEG = 8
UNROLL = 4
CENT_DEV = 256


kernel_scale = 0.6
ridge_shift = 0.1


def gaussian(left_feats, right_feats):
    inner = lax.dot_general(
        left_feats, right_feats, (((1,), (1,)), ((), ())), preferred_element_type=jnp.float32
    )
    left_norm = jnp.sum(jnp.square(left_feats.astype(jnp.float32)), axis=1)
    right_norm = jnp.sum(jnp.square(right_feats.astype(jnp.float32)), axis=1)
    feat_width = left_feats.shape[1]
    return jnp.exp(
        -(kernel_scale / feat_width) * (left_norm[:, None] + right_norm[None, :] - 2.0 * inner)
    )


def ridged(left_feats, left_index, right_feats, right_index):
    eye = (left_index[:, None] == right_index[None, :]).astype(jnp.float32)
    return gaussian(left_feats, right_feats) + ridge_shift * eye


def matmul_t(left, right):
    return lax.dot_general(
        left,
        right,
        (((1,), (1,)), ((), ())),
        precision=lax.Precision.HIGHEST,
        preferred_element_type=jnp.float32,
    )


def _dot_t(left, right):
    return lax.dot_general(
        left, right, (((1,), (1,)), ((), ())),
        precision=lax.Precision.HIGHEST, preferred_element_type=jnp.float32,
    )


def _factor_kernel(m_ref, blk_ref, p_ref, w_ref):
    rows, width = m_ref.shape
    n = BLOCK
    row_i = lax.broadcasted_iota(jnp.int32, (n, n), 0)
    col_i = lax.broadcasted_iota(jnp.int32, (n, n), 1)
    eye = jnp.where(row_i == col_i, 1.0, 0.0).astype(jnp.float32)
    lane_row = lax.broadcasted_iota(jnp.int32, (1, 2 * n), 1)

    def segment(start, piv):
        high = n - start
        sub_w = lax.broadcasted_iota(jnp.int32, (high, 2 * n), 0) + start
        sub_col = lax.broadcasted_iota(jnp.int32, (high, 1), 0) + start
        col_s = lax.broadcasted_iota(jnp.int32, (high, n), 1)

        def body(j, piv):
            w = w_ref[start:, :]
            rowj = w_ref[pl.ds(j, 1), :]
            jn = jnp.minimum(j + 1, n - 1)
            rown = w_ref[pl.ds(jn, 1), :]
            r = 1.0 / jnp.sqrt(piv)
            srow = rowj * r
            colj = jnp.sum(jnp.where(col_s == j, w[:, :n], 0.0), axis=1, keepdims=True)
            m = jnp.where(sub_col > j, colj * r, 0.0)
            w_ref[start:, :] = jnp.where(sub_w == j, srow, w - m * srow)
            a = jnp.sum(jnp.where(lane_row == jn, rown, 0.0), axis=1, keepdims=True)
            b = jnp.sum(jnp.where(lane_row == jn, rowj, 0.0), axis=1, keepdims=True) * r
            return a - b * b

        return lax.fori_loop(start, start + SEG, body, piv, unroll=UNROLL)

    for step in range(width // n):
        c0 = step * n
        diag = m_ref[c0 : c0 + n, c0 : c0 + n]
        diag = (diag + diag.T) * 0.5
        w_ref[:, :n] = diag
        w_ref[:, n:] = eye
        piv0 = jnp.sum(jnp.where(row_i[0:1] == col_i[0:1], diag[0:1], 0.0), axis=1, keepdims=True)
        piv = piv0
        for start in range(0, n, SEG):
            piv = segment(start, piv)
        w = w_ref[...]
        factor = jnp.where(col_i >= row_i, w[:, :n], 0.0).T
        inverse = jnp.where(col_i <= row_i, w[:, n:], 0.0)
        def solve_chunk(i, carry, c0=c0, step=step, factor=factor, inverse=inverse):
            r0 = pl.multiple_of(i * CHUNK, CHUNK)
            column = m_ref[pl.ds(r0, CHUNK), c0 : c0 + n]
            solved = _dot_t(column, inverse)
            blk = blk_ref[pl.ds(r0, CHUNK), :]
            tiled = jnp.concatenate([factor] * (CHUNK // n), axis=0)
            p_ref[pl.ds(r0, CHUNK), c0 : c0 + n] = jnp.where(
                blk > step, solved, jnp.where(blk == step, tiled, 0.0)
            )
            return carry

        lax.fori_loop(0, rows // CHUNK, solve_chunk, 0)
        if c0 + n < width:
            later = p_ref[c0 + n : width, c0 : c0 + n]

            def update_chunk(i, carry, c0=c0, later=later):
                r0 = pl.multiple_of(i * CHUNK, CHUNK)
                m_ref[pl.ds(r0, CHUNK), c0 + n : width] = m_ref[pl.ds(r0, CHUNK), c0 + n : width] - _dot_t(
                    p_ref[pl.ds(r0, CHUNK), c0 : c0 + n], later
                )
                return carry

            lax.fori_loop(0, rows // CHUNK, update_chunk, 0)


def factor_rows(kernel_rows, row_block):
    rows, width = kernel_rows.shape
    return pl.pallas_call(
        _factor_kernel,
        out_shape=jax.ShapeDtypeStruct((rows, width), jnp.float32),
        scratch_shapes=[pltpu.VMEM((BLOCK, 2 * BLOCK), jnp.float32)],
        input_output_aliases={},
    )(kernel_rows, row_block)


def tile_rows(tiles):
    return (tiles[:, None] * PANEL + jnp.arange(PANEL, dtype=jnp.int32)[None, :]).reshape(-1)


def per_device(frames, center_picks, send_counts, send_offsets):
    rows_axis = lax.axis_size("row")
    cols_axis = lax.axis_size("col")
    row_id = lax.axis_index("row")
    col_id = lax.axis_index("col")
    feat_width = frames.shape[1]
    capacity = center_picks.shape[2]
    outgoing = frames[center_picks[0]]
    incoming = lax.all_to_all(outgoing, "col", split_axis=0, concat_axis=0, tiled=True)
    position = jnp.arange(CENT_DEV, dtype=jnp.int32)
    starts = send_offsets[:, 0]
    lengths = send_counts[:, 0]
    inside = (position[:, None] >= starts[None, :]) & (
        position[:, None] < (starts + lengths)[None, :]
    )
    source = jnp.sum(jnp.where(inside, jnp.arange(cols_axis, dtype=jnp.int32)[None, :], 0), axis=1)
    within = position - jnp.sum(jnp.where(inside, starts[None, :], 0), axis=1)
    own_feats = incoming.reshape(cols_axis * capacity, feat_width)[source * capacity + within]
    col_slots = CENT_DEV // PANEL
    row_tiles_dev = col_slots * cols_axis // rows_axis
    gathered = lax.all_gather(own_feats, "col", axis=0, tiled=True)
    centers = (
        gathered.reshape(cols_axis, col_slots, PANEL, feat_width)
        .transpose(1, 0, 2, 3)
        .reshape(cols_axis * col_slots * PANEL, feat_width)
    )
    panel_tiles = jnp.arange(PANELS, dtype=jnp.int32)
    my_row_tiles = row_id + rows_axis * jnp.arange(row_tiles_dev, dtype=jnp.int32)
    my_col_tiles = col_id + cols_axis * jnp.arange(col_slots, dtype=jnp.int32)
    ext_tiles = jnp.concatenate([panel_tiles, my_row_tiles, my_col_tiles])
    ext_index = tile_rows(ext_tiles)
    panel_index = tile_rows(panel_tiles)
    ext_feats = jnp.concatenate(
        [centers[: PANELS * PANEL]]
        + [
            lax.dynamic_slice_in_dim(centers, tile * PANEL, PANEL, 0)
            for tile in list(my_row_tiles) + list(my_col_tiles)
        ],
        axis=0,
    )
    panel_feats = centers[: PANELS * PANEL]
    kernel = ridged(ext_feats, ext_index, panel_feats, panel_index)
    every_panel = factor_rows(kernel, (ext_index // BLOCK)[:, None])
    base = PANELS * PANEL
    rows_dev = row_tiles_dev * PANEL
    row_panel = every_panel[base : base + rows_dev]
    col_panel = every_panel[base + rows_dev :]
    row_index = ext_index[base : base + rows_dev]
    col_index = ext_index[base + rows_dev :]
    block = ridged(ext_feats[base : base + rows_dev], row_index, ext_feats[base + rows_dev :], col_index)
    trailing = (block - matmul_t(row_panel, col_panel)).reshape(1, rows_dev, 1, CENT_DEV)
    share_rows = rows_dev // cols_axis
    panel_share = lax.dynamic_slice_in_dim(row_panel, col_id * share_rows, share_rows, 0).reshape(
        1, share_rows, PANELS * PANEL
    )
    return (panel_share, trailing)


def solution(mesh):
    in_specs = (P("col", None), P("col", None, None), P(None, "col"), P(None, "col"))
    out_specs = (P("row", "col", None), P("row", None, "col", None))
    return jax.shard_map(
        per_device, mesh=mesh, in_specs=in_specs, out_specs=out_specs, check_vma=False
    )
```

```python
import functools

import jax
import jax.numpy as jnp
from jax import lax
from jax.experimental import pallas as pl
from jax.experimental.pallas import tpu as pltpu
from jax.sharding import PartitionSpec as P

PANEL = 256
PANELS = 4
BLOCK = 128
CHUNK = 256
SEG = 8
CENT_DEV = 256


kernel_scale = 0.6
ridge_shift = 0.1


def gaussian(left_feats, right_feats):
    inner = lax.dot_general(
        left_feats, right_feats, (((1,), (1,)), ((), ())), preferred_element_type=jnp.float32
    )
    left_norm = jnp.sum(jnp.square(left_feats.astype(jnp.float32)), axis=1)
    right_norm = jnp.sum(jnp.square(right_feats.astype(jnp.float32)), axis=1)
    feat_width = left_feats.shape[1]
    return jnp.exp(
        -(kernel_scale / feat_width) * (left_norm[:, None] + right_norm[None, :] - 2.0 * inner)
    )


def ridged(left_feats, left_index, right_feats, right_index):
    eye = (left_index[:, None] == right_index[None, :]).astype(jnp.float32)
    return gaussian(left_feats, right_feats) + ridge_shift * eye


def matmul_t(left, right):
    return lax.dot_general(
        left,
        right,
        (((1,), (1,)), ((), ())),
        precision=lax.Precision.HIGHEST,
        preferred_element_type=jnp.float32,
    )


def _dot_t(left, right):
    return lax.dot_general(
        left, right, (((1,), (1,)), ((), ())),
        precision=lax.Precision.HIGHEST, preferred_element_type=jnp.float32,
    )


def _factor_kernel(xf_ref, xsq_ref, idx_ref, pf_ref, psq_ref, out_ref, m_ref, p_ref, w_ref, *, feat_width):
    rows, width = m_ref.shape
    scale = kernel_scale / feat_width
    panel_feats = pf_ref[...]
    panel_sq = psq_ref[...]
    lane_cols = lax.broadcasted_iota(jnp.int32, (CHUNK, width), 1)
    for r0 in range(0, rows, CHUNK):
        inner = lax.dot_general(
            xf_ref[r0 : r0 + CHUNK, :], panel_feats, (((1,), (1,)), ((), ())),
            preferred_element_type=jnp.float32,
        )
        value = jnp.exp(-scale * (xsq_ref[r0 : r0 + CHUNK, :] + panel_sq - 2.0 * inner))
        eye = jnp.where(idx_ref[r0 : r0 + CHUNK, :] == lane_cols, 1.0, 0.0)
        m_ref[r0 : r0 + CHUNK, :] = value + ridge_shift * eye

    def panel_at(r0):
        return (p_ref, r0) if r0 < width else (out_ref, r0 - width)

    n = BLOCK
    row_i = lax.broadcasted_iota(jnp.int32, (n, n), 0)
    col_i = lax.broadcasted_iota(jnp.int32, (n, n), 1)
    eye = jnp.where(row_i == col_i, 1.0, 0.0).astype(jnp.float32)
    lane_row = lax.broadcasted_iota(jnp.int32, (1, 2 * n), 1)

    def segment(start, piv):
        high = n - start
        sub_w = lax.broadcasted_iota(jnp.int32, (high, 2 * n), 0) + start
        sub_col = lax.broadcasted_iota(jnp.int32, (high, 1), 0) + start
        col_s = lax.broadcasted_iota(jnp.int32, (high, n), 1)

        def body(j, piv):
            w = w_ref[start:, :]
            rowj = w_ref[pl.ds(j, 1), :]
            jn = jnp.minimum(j + 1, n - 1)
            rown = w_ref[pl.ds(jn, 1), :]
            r = 1.0 / jnp.sqrt(piv)
            srow = rowj * r
            colj = jnp.sum(jnp.where(col_s == j, w[:, :n], 0.0), axis=1, keepdims=True)
            m = jnp.where(sub_col > j, colj * r, 0.0)
            w_ref[start:, :] = jnp.where(sub_w == j, srow, w - m * srow)
            a = jnp.sum(jnp.where(lane_row == jn, rown, 0.0), axis=1, keepdims=True)
            b = jnp.sum(jnp.where(lane_row == jn, rowj, 0.0), axis=1, keepdims=True) * r
            return a - b * b

        return lax.fori_loop(start, start + SEG, body, piv, unroll=SEG)

    for step in range(width // n):
        c0 = step * n
        diag = m_ref[c0 : c0 + n, c0 : c0 + n]
        diag = (diag + diag.T) * 0.5
        w_ref[:, :n] = diag
        w_ref[:, n:] = eye
        piv0 = jnp.sum(jnp.where(row_i[0:1] == col_i[0:1], diag[0:1], 0.0), axis=1, keepdims=True)
        piv = piv0
        for start in range(0, n, SEG):
            piv = segment(start, piv)
        w = w_ref[...]
        factor = jnp.where(col_i >= row_i, w[:, :n], 0.0).T
        inverse = jnp.where(col_i <= row_i, w[:, n:], 0.0)
        for r0 in range(0, rows, CHUNK):
            column = m_ref[r0 : r0 + CHUNK, c0 : c0 + n]
            solved = _dot_t(column, inverse)
            idx = idx_ref[r0 : r0 + CHUNK, :]
            tiled = jnp.concatenate([factor] * (CHUNK // n), axis=0)
            here = jnp.where(idx >= c0, tiled, 0.0)
            ref, at = panel_at(r0)
            ref[at : at + CHUNK, c0 : c0 + n] = jnp.where(idx >= c0 + n, solved, here)
        if c0 + n < width:
            later = p_ref[c0 + n : width, c0 : c0 + n]
            for r0 in range(0, rows, CHUNK):
                ref, at = panel_at(r0)
                m_ref[r0 : r0 + CHUNK, c0 + n : width] = m_ref[r0 : r0 + CHUNK, c0 + n : width] - _dot_t(
                    ref[at : at + CHUNK, c0 : c0 + n], later
                )


def factor_rows(ext_feats, ext_index, panel_feats):
    rows = ext_feats.shape[0]
    width = panel_feats.shape[0]
    pad = (-ext_feats.shape[1]) % 128
    ext_sq = jnp.sum(jnp.square(ext_feats.astype(jnp.float32)), axis=1)[:, None]
    panel_sq = jnp.sum(jnp.square(panel_feats.astype(jnp.float32)), axis=1)[None, :]
    return pl.pallas_call(
        functools.partial(_factor_kernel, feat_width=ext_feats.shape[1]),
        out_shape=jax.ShapeDtypeStruct((rows - width, width), jnp.float32),
        scratch_shapes=[
            pltpu.VMEM((rows, width), jnp.float32),
            pltpu.VMEM((width, width), jnp.float32),
            pltpu.VMEM((BLOCK, 2 * BLOCK), jnp.float32),
        ],
    )(
        jnp.pad(ext_feats, ((0, 0), (0, pad))),
        ext_sq,
        ext_index[:, None],
        jnp.pad(panel_feats, ((0, 0), (0, pad))),
        panel_sq,
    )


def tile_rows(tiles):
    return (tiles[:, None] * PANEL + jnp.arange(PANEL, dtype=jnp.int32)[None, :]).reshape(-1)


def per_device(frames, center_picks, send_counts, send_offsets):
    rows_axis = lax.axis_size("row")
    cols_axis = lax.axis_size("col")
    row_id = lax.axis_index("row")
    col_id = lax.axis_index("col")
    feat_width = frames.shape[1]
    capacity = center_picks.shape[2]
    outgoing = frames[center_picks[0]]
    incoming = lax.all_to_all(outgoing, "col", split_axis=0, concat_axis=0, tiled=True)
    position = jnp.arange(CENT_DEV, dtype=jnp.int32)
    starts = send_offsets[:, 0]
    lengths = send_counts[:, 0]
    inside = (position[:, None] >= starts[None, :]) & (
        position[:, None] < (starts + lengths)[None, :]
    )
    source = jnp.sum(jnp.where(inside, jnp.arange(cols_axis, dtype=jnp.int32)[None, :], 0), axis=1)
    within = position - jnp.sum(jnp.where(inside, starts[None, :], 0), axis=1)
    own_feats = incoming.reshape(cols_axis * capacity, feat_width)[source * capacity + within]
    col_slots = CENT_DEV // PANEL
    row_tiles_dev = col_slots * cols_axis // rows_axis
    gathered = lax.all_gather(own_feats, "col", axis=0, tiled=True)
    centers = (
        gathered.reshape(cols_axis, col_slots, PANEL, feat_width)
        .transpose(1, 0, 2, 3)
        .reshape(cols_axis * col_slots * PANEL, feat_width)
    )
    panel_tiles = jnp.arange(PANELS, dtype=jnp.int32)
    my_row_tiles = row_id + rows_axis * jnp.arange(row_tiles_dev, dtype=jnp.int32)
    my_col_tiles = col_id + cols_axis * jnp.arange(col_slots, dtype=jnp.int32)
    ext_tiles = jnp.concatenate([panel_tiles, my_row_tiles, my_col_tiles])
    ext_index = tile_rows(ext_tiles)
    panel_index = tile_rows(panel_tiles)
    ext_feats = jnp.concatenate(
        [centers[: PANELS * PANEL]]
        + [
            lax.dynamic_slice_in_dim(centers, tile * PANEL, PANEL, 0)
            for tile in list(my_row_tiles) + list(my_col_tiles)
        ],
        axis=0,
    )
    panel_feats = centers[: PANELS * PANEL]
    extra_panel = factor_rows(ext_feats, ext_index, panel_feats)
    base = PANELS * PANEL
    rows_dev = row_tiles_dev * PANEL
    row_panel = extra_panel[:rows_dev]
    col_panel = extra_panel[rows_dev:]
    row_index = ext_index[base : base + rows_dev]
    col_index = ext_index[base + rows_dev :]
    block = ridged(ext_feats[base : base + rows_dev], row_index, ext_feats[base + rows_dev :], col_index)
    trailing = (block - matmul_t(row_panel, col_panel)).reshape(1, rows_dev, 1, CENT_DEV)
    share_rows = rows_dev // cols_axis
    panel_share = lax.dynamic_slice_in_dim(row_panel, col_id * share_rows, share_rows, 0).reshape(
        1, share_rows, PANELS * PANEL
    )
    return (panel_share, trailing)


def solution(mesh):
    in_specs = (P("col", None), P("col", None, None), P(None, "col"), P(None, "col"))
    out_specs = (P("row", "col", None), P("row", None, "col", None))
    return jax.shard_map(
        per_device, mesh=mesh, in_specs=in_specs, out_specs=out_specs, check_vma=False
    )
```

```python
import functools

import jax
import jax.numpy as jnp
from jax import lax
from jax.experimental import pallas as pl
from jax.experimental.pallas import tpu as pltpu
from jax.sharding import PartitionSpec as P

PANEL = 256
PANELS = 4
BLOCK = 128
CHUNK = 256
SEG = 8
CENT_DEV = 256


kernel_scale = 0.6
ridge_shift = 0.1


def gaussian(left_feats, right_feats):
    inner = lax.dot_general(
        left_feats, right_feats, (((1,), (1,)), ((), ())), preferred_element_type=jnp.float32
    )
    left_norm = jnp.sum(jnp.square(left_feats.astype(jnp.float32)), axis=1)
    right_norm = jnp.sum(jnp.square(right_feats.astype(jnp.float32)), axis=1)
    feat_width = left_feats.shape[1]
    return jnp.exp(
        -(kernel_scale / feat_width) * (left_norm[:, None] + right_norm[None, :] - 2.0 * inner)
    )


def ridged(left_feats, left_index, right_feats, right_index):
    eye = (left_index[:, None] == right_index[None, :]).astype(jnp.float32)
    return gaussian(left_feats, right_feats) + ridge_shift * eye


def matmul_t(left, right):
    return lax.dot_general(
        left,
        right,
        (((1,), (1,)), ((), ())),
        precision=lax.Precision.HIGHEST,
        preferred_element_type=jnp.float32,
    )


def _dot_t(left, right):
    return lax.dot_general(
        left, right, (((1,), (1,)), ((), ())),
        precision=lax.Precision.HIGHEST, preferred_element_type=jnp.float32,
    )


def _factor_kernel(xf_ref, xsq_ref, idx_ref, pf_ref, psq_ref, out_ref, m_ref, p_ref, w_ref, *, feat_width):
    rows, width = m_ref.shape
    scale = kernel_scale / feat_width
    panel_feats = pf_ref[...]
    panel_sq = psq_ref[...]
    lane_cols = lax.broadcasted_iota(jnp.int32, (CHUNK, width), 1)
    for r0 in range(0, rows, CHUNK):
        inner = lax.dot_general(
            xf_ref[r0 : r0 + CHUNK, :], panel_feats, (((1,), (1,)), ((), ())),
            preferred_element_type=jnp.float32,
        )
        value = jnp.exp(-scale * (xsq_ref[r0 : r0 + CHUNK, :] + panel_sq - 2.0 * inner))
        eye = jnp.where(idx_ref[r0 : r0 + CHUNK, :] == lane_cols, 1.0, 0.0)
        m_ref[r0 : r0 + CHUNK, :] = value + ridge_shift * eye

    def panel_at(r0):
        return (p_ref, r0) if r0 < width else (out_ref, r0 - width)

    n = BLOCK
    row_i = lax.broadcasted_iota(jnp.int32, (n, n), 0)
    col_i = lax.broadcasted_iota(jnp.int32, (n, n), 1)
    eye = jnp.where(row_i == col_i, 1.0, 0.0).astype(jnp.float32)
    lane_row = lax.broadcasted_iota(jnp.int32, (1, 2 * n), 1)

    def segment(start, piv):
        high = n - start
        sub_w = lax.broadcasted_iota(jnp.int32, (high, 2 * n), 0) + start
        sub_col = lax.broadcasted_iota(jnp.int32, (high, 1), 0) + start
        col_s = lax.broadcasted_iota(jnp.int32, (high, n), 1)

        def body(j, piv):
            w = w_ref[start:, :]
            rowj = w_ref[pl.ds(j, 1), :]
            jn = jnp.minimum(j + 1, n - 1)
            rown = w_ref[pl.ds(jn, 1), :]
            r = 1.0 / jnp.sqrt(piv)
            srow = rowj * r
            colj = jnp.sum(jnp.where(col_s == j, w[:, :n], 0.0), axis=1, keepdims=True)
            m = jnp.where(sub_col > j, colj * r, 0.0)
            w_ref[start:, :] = jnp.where(sub_w == j, srow, w - m * srow)
            a = jnp.sum(jnp.where(lane_row == jn, rown, 0.0), axis=1, keepdims=True)
            b = jnp.sum(jnp.where(lane_row == jn, rowj, 0.0), axis=1, keepdims=True) * r
            return a - b * b

        return lax.fori_loop(start, start + SEG, body, piv, unroll=SEG)

    for step in range(width // n):
        c0 = step * n
        diag = m_ref[c0 : c0 + n, c0 : c0 + n]
        diag = (diag + diag.T) * 0.5
        w_ref[:, :n] = diag
        w_ref[:, n:] = eye
        piv0 = jnp.sum(jnp.where(row_i[0:1] == col_i[0:1], diag[0:1], 0.0), axis=1, keepdims=True)
        piv = piv0
        for start in range(0, n, SEG):
            piv = segment(start, piv)
        w = w_ref[...]
        factor = jnp.where(col_i >= row_i, w[:, :n], 0.0).T
        inverse = jnp.where(col_i <= row_i, w[:, n:], 0.0)
        for r0 in range(0, rows, CHUNK):
            column = m_ref[r0 : r0 + CHUNK, c0 : c0 + n]
            solved = _dot_t(column, inverse)
            idx = idx_ref[r0 : r0 + CHUNK, :]
            tiled = jnp.concatenate([factor] * (CHUNK // n), axis=0)
            here = jnp.where(idx >= c0, tiled, 0.0)
            ref, at = panel_at(r0)
            ref[at : at + CHUNK, c0 : c0 + n] = jnp.where(idx >= c0 + n, solved, here)
        if c0 + n < width:
            later = p_ref[c0 + n : width, c0 : c0 + n]
            for r0 in range(0, rows, CHUNK):
                ref, at = panel_at(r0)
                m_ref[r0 : r0 + CHUNK, c0 + n : width] = m_ref[r0 : r0 + CHUNK, c0 + n : width] - _dot_t(
                    ref[at : at + CHUNK, c0 : c0 + n], later
                )


def factor_rows(ext_feats, ext_index, panel_feats):
    rows = ext_feats.shape[0]
    width = panel_feats.shape[0]
    pad = (-ext_feats.shape[1]) % 128
    ext_sq = jnp.sum(jnp.square(ext_feats.astype(jnp.float32)), axis=1)[:, None]
    panel_sq = jnp.sum(jnp.square(panel_feats.astype(jnp.float32)), axis=1)[None, :]
    return pl.pallas_call(
        functools.partial(_factor_kernel, feat_width=ext_feats.shape[1]),
        out_shape=jax.ShapeDtypeStruct((rows - width, width), jnp.float32),
        scratch_shapes=[
            pltpu.VMEM((rows, width), jnp.float32),
            pltpu.VMEM((width, width), jnp.float32),
            pltpu.VMEM((BLOCK, 2 * BLOCK), jnp.float32),
        ],
    )(
        jnp.pad(ext_feats, ((0, 0), (0, pad))),
        ext_sq,
        ext_index[:, None],
        jnp.pad(panel_feats, ((0, 0), (0, pad))),
        panel_sq,
    )


def tile_rows(tiles):
    return (tiles[:, None] * PANEL + jnp.arange(PANEL, dtype=jnp.int32)[None, :]).reshape(-1)


def per_device(frames, center_picks, send_counts, send_offsets):
    rows_axis = lax.axis_size("row")
    cols_axis = lax.axis_size("col")
    row_id = lax.axis_index("row")
    col_id = lax.axis_index("col")
    feat_width = frames.shape[1]
    capacity = center_picks.shape[2]
    outgoing = frames[center_picks[0]]
    incoming = lax.all_to_all(outgoing, "col", split_axis=0, concat_axis=0, tiled=True)
    position = jnp.arange(CENT_DEV, dtype=jnp.int32)
    starts = send_offsets[:, 0]
    lengths = send_counts[:, 0]
    inside = (position[:, None] >= starts[None, :]) & (
        position[:, None] < (starts + lengths)[None, :]
    )
    source = jnp.sum(jnp.where(inside, jnp.arange(cols_axis, dtype=jnp.int32)[None, :], 0), axis=1)
    within = position - jnp.sum(jnp.where(inside, starts[None, :], 0), axis=1)
    own_feats = incoming.reshape(cols_axis * capacity, feat_width)[source * capacity + within]
    col_slots = CENT_DEV // PANEL
    row_tiles_dev = col_slots * cols_axis // rows_axis
    copies = jnp.broadcast_to(own_feats[None], (cols_axis,) + own_feats.shape)
    gathered = lax.all_to_all(copies, "col", split_axis=0, concat_axis=0, tiled=True)
    centers = (
        gathered.reshape(cols_axis, col_slots, PANEL, feat_width)
        .transpose(1, 0, 2, 3)
        .reshape(cols_axis * col_slots * PANEL, feat_width)
    )
    panel_tiles = jnp.arange(PANELS, dtype=jnp.int32)
    my_row_tiles = row_id + rows_axis * jnp.arange(row_tiles_dev, dtype=jnp.int32)
    my_col_tiles = col_id + cols_axis * jnp.arange(col_slots, dtype=jnp.int32)
    ext_tiles = jnp.concatenate([panel_tiles, my_row_tiles, my_col_tiles])
    ext_index = tile_rows(ext_tiles)
    panel_index = tile_rows(panel_tiles)
    ext_feats = jnp.concatenate(
        [centers[: PANELS * PANEL]]
        + [
            lax.dynamic_slice_in_dim(centers, tile * PANEL, PANEL, 0)
            for tile in list(my_row_tiles) + list(my_col_tiles)
        ],
        axis=0,
    )
    panel_feats = centers[: PANELS * PANEL]
    extra_panel = factor_rows(ext_feats, ext_index, panel_feats)
    base = PANELS * PANEL
    rows_dev = row_tiles_dev * PANEL
    row_panel = extra_panel[:rows_dev]
    col_panel = extra_panel[rows_dev:]
    row_index = ext_index[base : base + rows_dev]
    col_index = ext_index[base + rows_dev :]
    block = ridged(ext_feats[base : base + rows_dev], row_index, ext_feats[base + rows_dev :], col_index)
    trailing = (block - matmul_t(row_panel, col_panel)).reshape(1, rows_dev, 1, CENT_DEV)
    share_rows = rows_dev // cols_axis
    panel_share = lax.dynamic_slice_in_dim(row_panel, col_id * share_rows, share_rows, 0).reshape(
        1, share_rows, PANELS * PANEL
    )
    return (panel_share, trailing)


def solution(mesh):
    in_specs = (P("col", None), P("col", None, None), P(None, "col"), P(None, "col"))
    out_specs = (P("row", "col", None), P("row", None, "col", None))
    return jax.shard_map(
        per_device, mesh=mesh, in_specs=in_specs, out_specs=out_specs, check_vma=False
    )
```

```python
import functools

import jax
import jax.numpy as jnp
from jax import lax
from jax.experimental import pallas as pl
from jax.experimental.pallas import tpu as pltpu
from jax.sharding import PartitionSpec as P

PANEL = 256
PANELS = 4
BLOCK = 128
CHUNK = 256
SEG = 8
CENT_DEV = 256


kernel_scale = 0.6
ridge_shift = 0.1


def gaussian(left_feats, right_feats):
    inner = lax.dot_general(
        left_feats, right_feats, (((1,), (1,)), ((), ())), preferred_element_type=jnp.float32
    )
    left_norm = jnp.sum(jnp.square(left_feats.astype(jnp.float32)), axis=1)
    right_norm = jnp.sum(jnp.square(right_feats.astype(jnp.float32)), axis=1)
    feat_width = left_feats.shape[1]
    return jnp.exp(
        -(kernel_scale / feat_width) * (left_norm[:, None] + right_norm[None, :] - 2.0 * inner)
    )


def ridged(left_feats, left_index, right_feats, right_index):
    eye = (left_index[:, None] == right_index[None, :]).astype(jnp.float32)
    return gaussian(left_feats, right_feats) + ridge_shift * eye


def matmul_t(left, right):
    return lax.dot_general(
        left,
        right,
        (((1,), (1,)), ((), ())),
        precision=lax.Precision.HIGHEST,
        preferred_element_type=jnp.float32,
    )


def _dot_t(left, right):
    return lax.dot_general(
        left, right, (((1,), (1,)), ((), ())),
        precision=lax.Precision.HIGHEST, preferred_element_type=jnp.float32,
    )


def _factor_kernel(xf_ref, xsq_ref, idx_ref, psq_ref, out_ref, m_ref, p_ref, w_ref, *, feat_width):
    rows, width = m_ref.shape
    scale = kernel_scale / feat_width
    panel_feats = xf_ref[0:width, :]
    panel_sq = psq_ref[...]
    lane_cols = lax.broadcasted_iota(jnp.int32, (CHUNK, width), 1)
    for r0 in range(0, rows, CHUNK):
        inner = lax.dot_general(
            xf_ref[r0 : r0 + CHUNK, :], panel_feats, (((1,), (1,)), ((), ())),
            preferred_element_type=jnp.float32,
        )
        value = jnp.exp(-scale * (xsq_ref[r0 : r0 + CHUNK, :] + panel_sq - 2.0 * inner))
        eye = jnp.where(idx_ref[r0 : r0 + CHUNK, :] == lane_cols, 1.0, 0.0)
        m_ref[r0 : r0 + CHUNK, :] = value + ridge_shift * eye

    def panel_at(r0):
        return (p_ref, r0) if r0 < width else (out_ref, r0 - width)

    n = BLOCK
    row_i = lax.broadcasted_iota(jnp.int32, (n, n), 0)
    col_i = lax.broadcasted_iota(jnp.int32, (n, n), 1)
    eye = jnp.where(row_i == col_i, 1.0, 0.0).astype(jnp.float32)
    lane_row = lax.broadcasted_iota(jnp.int32, (1, 2 * n), 1)

    def segment(start, piv):
        high = n - start
        sub_w = lax.broadcasted_iota(jnp.int32, (high, 2 * n), 0) + start
        sub_col = lax.broadcasted_iota(jnp.int32, (high, 1), 0) + start
        col_s = lax.broadcasted_iota(jnp.int32, (high, n), 1)

        def body(j, piv):
            w = w_ref[start:, :]
            rowj = w_ref[pl.ds(j, 1), :]
            jn = jnp.minimum(j + 1, n - 1)
            rown = w_ref[pl.ds(jn, 1), :]
            r = 1.0 / jnp.sqrt(piv)
            srow = rowj * r
            colj = jnp.sum(jnp.where(col_s == j, w[:, :n], 0.0), axis=1, keepdims=True)
            m = jnp.where(sub_col > j, colj * r, 0.0)
            w_ref[start:, :] = jnp.where(sub_w == j, srow, w - m * srow)
            a = jnp.sum(jnp.where(lane_row == jn, rown, 0.0), axis=1, keepdims=True)
            b = jnp.sum(jnp.where(lane_row == jn, rowj, 0.0), axis=1, keepdims=True) * r
            return a - b * b

        return lax.fori_loop(start, start + SEG, body, piv, unroll=SEG)

    for step in range(width // n):
        c0 = step * n
        diag = m_ref[c0 : c0 + n, c0 : c0 + n]
        diag = (diag + diag.T) * 0.5
        w_ref[:, :n] = diag
        w_ref[:, n:] = eye
        piv0 = jnp.sum(jnp.where(row_i[0:1] == col_i[0:1], diag[0:1], 0.0), axis=1, keepdims=True)
        piv = piv0
        for start in range(0, n, SEG):
            piv = segment(start, piv)
        w = w_ref[...]
        factor = jnp.where(col_i >= row_i, w[:, :n], 0.0).T
        inverse = jnp.where(col_i <= row_i, w[:, n:], 0.0)
        for r0 in range(0, rows, CHUNK):
            column = m_ref[r0 : r0 + CHUNK, c0 : c0 + n]
            solved = _dot_t(column, inverse)
            idx = idx_ref[r0 : r0 + CHUNK, :]
            tiled = jnp.concatenate([factor] * (CHUNK // n), axis=0)
            here = jnp.where(idx >= c0, tiled, 0.0)
            ref, at = panel_at(r0)
            ref[at : at + CHUNK, c0 : c0 + n] = jnp.where(idx >= c0 + n, solved, here)
        if c0 + n < width:
            later = p_ref[c0 + n : width, c0 : c0 + n]
            for r0 in range(0, rows, CHUNK):
                ref, at = panel_at(r0)
                m_ref[r0 : r0 + CHUNK, c0 + n : width] = m_ref[r0 : r0 + CHUNK, c0 + n : width] - _dot_t(
                    ref[at : at + CHUNK, c0 : c0 + n], later
                )


def factor_rows(ext_feats, ext_index, width):
    rows = ext_feats.shape[0]
    pad = (-ext_feats.shape[1]) % 128
    ext_sq = jnp.sum(jnp.square(ext_feats.astype(jnp.float32)), axis=1)
    return pl.pallas_call(
        functools.partial(_factor_kernel, feat_width=ext_feats.shape[1]),
        out_shape=jax.ShapeDtypeStruct((rows - width, width), jnp.float32),
        scratch_shapes=[
            pltpu.VMEM((rows, width), jnp.float32),
            pltpu.VMEM((width, width), jnp.float32),
            pltpu.VMEM((BLOCK, 2 * BLOCK), jnp.float32),
        ],
    )(
        jnp.pad(ext_feats, ((0, 0), (0, pad))),
        ext_sq[:, None],
        ext_index[:, None],
        ext_sq[None, :width],
    )


def tile_rows(tiles):
    return (tiles[:, None] * PANEL + jnp.arange(PANEL, dtype=jnp.int32)[None, :]).reshape(-1)


def per_device(frames, center_picks, send_counts, send_offsets):
    rows_axis = lax.axis_size("row")
    cols_axis = lax.axis_size("col")
    row_id = lax.axis_index("row")
    col_id = lax.axis_index("col")
    feat_width = frames.shape[1]
    capacity = center_picks.shape[2]
    outgoing = frames[center_picks[0]]
    incoming = lax.all_to_all(outgoing, "col", split_axis=0, concat_axis=0, tiled=True)
    position = jnp.arange(CENT_DEV, dtype=jnp.int32)
    starts = send_offsets[:, 0]
    lengths = send_counts[:, 0]
    inside = (position[:, None] >= starts[None, :]) & (
        position[:, None] < (starts + lengths)[None, :]
    )
    source = jnp.sum(jnp.where(inside, jnp.arange(cols_axis, dtype=jnp.int32)[None, :], 0), axis=1)
    within = position - jnp.sum(jnp.where(inside, starts[None, :], 0), axis=1)
    own_feats = incoming.reshape(cols_axis * capacity, feat_width)[source * capacity + within]
    col_slots = CENT_DEV // PANEL
    row_tiles_dev = col_slots * cols_axis // rows_axis
    gathered = lax.all_gather(own_feats, "col", axis=0, tiled=True)
    centers = (
        gathered.reshape(cols_axis, col_slots, PANEL, feat_width)
        .transpose(1, 0, 2, 3)
        .reshape(cols_axis * col_slots * PANEL, feat_width)
    )
    panel_tiles = jnp.arange(PANELS, dtype=jnp.int32)
    my_row_tiles = row_id + rows_axis * jnp.arange(row_tiles_dev, dtype=jnp.int32)
    my_col_tiles = col_id + cols_axis * jnp.arange(col_slots, dtype=jnp.int32)
    ext_tiles = jnp.concatenate([panel_tiles, my_row_tiles, my_col_tiles])
    ext_index = tile_rows(ext_tiles)
    panel_index = tile_rows(panel_tiles)
    ext_feats = jnp.concatenate(
        [centers[: PANELS * PANEL]]
        + [
            lax.dynamic_slice_in_dim(centers, tile * PANEL, PANEL, 0)
            for tile in list(my_row_tiles) + list(my_col_tiles)
        ],
        axis=0,
    )
    extra_panel = factor_rows(ext_feats, ext_index, PANELS * PANEL)
    base = PANELS * PANEL
    rows_dev = row_tiles_dev * PANEL
    row_panel = extra_panel[:rows_dev]
    col_panel = extra_panel[rows_dev:]
    row_index = ext_index[base : base + rows_dev]
    col_index = ext_index[base + rows_dev :]
    block = ridged(ext_feats[base : base + rows_dev], row_index, ext_feats[base + rows_dev :], col_index)
    trailing = (block - matmul_t(row_panel, col_panel)).reshape(1, rows_dev, 1, CENT_DEV)
    share_rows = rows_dev // cols_axis
    panel_share = lax.dynamic_slice_in_dim(row_panel, col_id * share_rows, share_rows, 0).reshape(
        1, share_rows, PANELS * PANEL
    )
    return (panel_share, trailing)


def solution(mesh):
    in_specs = (P("col", None), P("col", None, None), P(None, "col"), P(None, "col"))
    out_specs = (P("row", "col", None), P("row", None, "col", None))
    return jax.shard_map(
        per_device, mesh=mesh, in_specs=in_specs, out_specs=out_specs, check_vma=False
    )
```

```python
import functools

import jax
import jax.numpy as jnp
from jax import lax
from jax.experimental import pallas as pl
from jax.experimental.pallas import tpu as pltpu
from jax.sharding import PartitionSpec as P

PANEL = 256
PANELS = 4
BLOCK = 128
CHUNK = 256
SEG = 8
CENT_DEV = 256


kernel_scale = 0.6
ridge_shift = 0.1


def gaussian(left_feats, right_feats):
    inner = lax.dot_general(
        left_feats, right_feats, (((1,), (1,)), ((), ())), preferred_element_type=jnp.float32
    )
    left_norm = jnp.sum(jnp.square(left_feats.astype(jnp.float32)), axis=1)
    right_norm = jnp.sum(jnp.square(right_feats.astype(jnp.float32)), axis=1)
    feat_width = left_feats.shape[1]
    return jnp.exp(
        -(kernel_scale / feat_width) * (left_norm[:, None] + right_norm[None, :] - 2.0 * inner)
    )


def ridged(left_feats, left_index, right_feats, right_index):
    eye = (left_index[:, None] == right_index[None, :]).astype(jnp.float32)
    return gaussian(left_feats, right_feats) + ridge_shift * eye


def matmul_t(left, right):
    return lax.dot_general(
        left,
        right,
        (((1,), (1,)), ((), ())),
        precision=lax.Precision.HIGHEST,
        preferred_element_type=jnp.float32,
    )


def _dot_t(left, right):
    return lax.dot_general(
        left, right, (((1,), (1,)), ((), ())),
        precision=lax.Precision.HIGHEST, preferred_element_type=jnp.float32,
    )


def _factor_kernel(xf_ref, xsq_ref, idx_ref, psq_ref, out_ref, m_ref, p_ref, w_ref, *, feat_width):
    rows, width = m_ref.shape
    scale = kernel_scale / feat_width
    panel_feats = xf_ref[0:width, :]
    panel_sq = psq_ref[...]
    lane_cols = lax.broadcasted_iota(jnp.int32, (CHUNK, width), 1)
    for r0 in range(0, rows, CHUNK):
        inner = lax.dot_general(
            xf_ref[r0 : r0 + CHUNK, :], panel_feats, (((1,), (1,)), ((), ())),
            preferred_element_type=jnp.float32,
        )
        value = jnp.exp(-scale * (xsq_ref[r0 : r0 + CHUNK, :] + panel_sq - 2.0 * inner))
        eye = jnp.where(idx_ref[r0 : r0 + CHUNK, :] == lane_cols, 1.0, 0.0)
        m_ref[r0 : r0 + CHUNK, :] = value + ridge_shift * eye

    def panel_at(r0):
        return (p_ref, r0) if r0 < width else (out_ref, r0 - width)

    n = BLOCK
    row_i = lax.broadcasted_iota(jnp.int32, (n, n), 0)
    col_i = lax.broadcasted_iota(jnp.int32, (n, n), 1)
    eye = jnp.where(row_i == col_i, 1.0, 0.0).astype(jnp.float32)
    lane_row = lax.broadcasted_iota(jnp.int32, (1, 2 * n), 1)

    def segment(start, piv):
        high = n - start
        sub_w = lax.broadcasted_iota(jnp.int32, (high, 2 * n), 0) + start
        sub_col = lax.broadcasted_iota(jnp.int32, (high, 1), 0) + start
        col_s = lax.broadcasted_iota(jnp.int32, (high, n), 1)

        def body(j, piv):
            w = w_ref[start:, :]
            rowj = w_ref[pl.ds(j, 1), :]
            jn = jnp.minimum(j + 1, n - 1)
            rown = w_ref[pl.ds(jn, 1), :]
            r = 1.0 / jnp.sqrt(piv)
            srow = rowj * r
            colj = jnp.sum(jnp.where(col_s == j, w[:, :n], 0.0), axis=1, keepdims=True)
            m = jnp.where(sub_col > j, colj * r, 0.0)
            w_ref[start:, :] = jnp.where(sub_w == j, srow, w - m * srow)
            a = jnp.sum(jnp.where(lane_row == jn, rown, 0.0), axis=1, keepdims=True)
            b = jnp.sum(jnp.where(lane_row == jn, rowj, 0.0), axis=1, keepdims=True) * r
            return a - b * b

        return lax.fori_loop(start, start + SEG, body, piv, unroll=SEG)

    for step in range(width // n):
        c0 = step * n
        diag = m_ref[c0 : c0 + n, c0 : c0 + n]
        diag = (diag + diag.T) * 0.5
        w_ref[:, :n] = diag
        w_ref[:, n:] = eye
        piv0 = jnp.sum(jnp.where(row_i[0:1] == col_i[0:1], diag[0:1], 0.0), axis=1, keepdims=True)
        piv = piv0
        for start in range(0, n, SEG):
            piv = segment(start, piv)
        w = w_ref[...]
        factor = jnp.where(col_i >= row_i, w[:, :n], 0.0).T
        inverse = jnp.where(col_i <= row_i, w[:, n:], 0.0)
        for r0 in range(0, rows, CHUNK):
            if r0 + CHUNK <= min(c0, width):
                p_ref[r0 : r0 + CHUNK, c0 : c0 + n] = jnp.zeros((CHUNK, n), jnp.float32)
                continue
            column = m_ref[r0 : r0 + CHUNK, c0 : c0 + n]
            solved = _dot_t(column, inverse)
            idx = idx_ref[r0 : r0 + CHUNK, :]
            tiled = jnp.concatenate([factor] * (CHUNK // n), axis=0)
            here = jnp.where(idx >= c0, tiled, 0.0)
            ref, at = panel_at(r0)
            ref[at : at + CHUNK, c0 : c0 + n] = jnp.where(idx >= c0 + n, solved, here)
        if c0 + n < width:
            later = p_ref[c0 + n : width, c0 : c0 + n]
            for r0 in range(0, rows, CHUNK):
                if r0 + CHUNK <= min(c0, width):
                    continue
                ref, at = panel_at(r0)
                m_ref[r0 : r0 + CHUNK, c0 + n : width] = m_ref[r0 : r0 + CHUNK, c0 + n : width] - _dot_t(
                    ref[at : at + CHUNK, c0 : c0 + n], later
                )


def factor_rows(ext_feats, ext_index, width):
    rows = ext_feats.shape[0]
    pad = (-ext_feats.shape[1]) % 128
    ext_sq = jnp.sum(jnp.square(ext_feats.astype(jnp.float32)), axis=1)
    return pl.pallas_call(
        functools.partial(_factor_kernel, feat_width=ext_feats.shape[1]),
        out_shape=jax.ShapeDtypeStruct((rows - width, width), jnp.float32),
        scratch_shapes=[
            pltpu.VMEM((rows, width), jnp.float32),
            pltpu.VMEM((width, width), jnp.float32),
            pltpu.VMEM((BLOCK, 2 * BLOCK), jnp.float32),
        ],
    )(
        jnp.pad(ext_feats, ((0, 0), (0, pad))),
        ext_sq[:, None],
        ext_index[:, None],
        ext_sq[None, :width],
    )


def tile_rows(tiles):
    return (tiles[:, None] * PANEL + jnp.arange(PANEL, dtype=jnp.int32)[None, :]).reshape(-1)


def per_device(frames, center_picks, send_counts, send_offsets):
    rows_axis = lax.axis_size("row")
    cols_axis = lax.axis_size("col")
    row_id = lax.axis_index("row")
    col_id = lax.axis_index("col")
    feat_width = frames.shape[1]
    capacity = center_picks.shape[2]
    outgoing = frames[center_picks[0]]
    incoming = lax.all_to_all(outgoing, "col", split_axis=0, concat_axis=0, tiled=True)
    position = jnp.arange(CENT_DEV, dtype=jnp.int32)
    starts = send_offsets[:, 0]
    lengths = send_counts[:, 0]
    inside = (position[:, None] >= starts[None, :]) & (
        position[:, None] < (starts + lengths)[None, :]
    )
    source = jnp.sum(jnp.where(inside, jnp.arange(cols_axis, dtype=jnp.int32)[None, :], 0), axis=1)
    within = position - jnp.sum(jnp.where(inside, starts[None, :], 0), axis=1)
    own_feats = incoming.reshape(cols_axis * capacity, feat_width)[source * capacity + within]
    col_slots = CENT_DEV // PANEL
    row_tiles_dev = col_slots * cols_axis // rows_axis
    gathered = lax.all_gather(own_feats, "col", axis=0, tiled=True)
    centers = (
        gathered.reshape(cols_axis, col_slots, PANEL, feat_width)
        .transpose(1, 0, 2, 3)
        .reshape(cols_axis * col_slots * PANEL, feat_width)
    )
    panel_tiles = jnp.arange(PANELS, dtype=jnp.int32)
    my_row_tiles = row_id + rows_axis * jnp.arange(row_tiles_dev, dtype=jnp.int32)
    my_col_tiles = col_id + cols_axis * jnp.arange(col_slots, dtype=jnp.int32)
    ext_tiles = jnp.concatenate([panel_tiles, my_row_tiles, my_col_tiles])
    ext_index = tile_rows(ext_tiles)
    panel_index = tile_rows(panel_tiles)
    ext_feats = jnp.concatenate(
        [centers[: PANELS * PANEL]]
        + [
            lax.dynamic_slice_in_dim(centers, tile * PANEL, PANEL, 0)
            for tile in list(my_row_tiles) + list(my_col_tiles)
        ],
        axis=0,
    )
    extra_panel = factor_rows(ext_feats, ext_index, PANELS * PANEL)
    base = PANELS * PANEL
    rows_dev = row_tiles_dev * PANEL
    row_panel = extra_panel[:rows_dev]
    col_panel = extra_panel[rows_dev:]
    row_index = ext_index[base : base + rows_dev]
    col_index = ext_index[base + rows_dev :]
    block = ridged(ext_feats[base : base + rows_dev], row_index, ext_feats[base + rows_dev :], col_index)
    trailing = (block - matmul_t(row_panel, col_panel)).reshape(1, rows_dev, 1, CENT_DEV)
    share_rows = rows_dev // cols_axis
    panel_share = lax.dynamic_slice_in_dim(row_panel, col_id * share_rows, share_rows, 0).reshape(
        1, share_rows, PANELS * PANEL
    )
    return (panel_share, trailing)


def solution(mesh):
    in_specs = (P("col", None), P("col", None, None), P(None, "col"), P(None, "col"))
    out_specs = (P("row", "col", None), P("row", None, "col", None))
    return jax.shard_map(
        per_device, mesh=mesh, in_specs=in_specs, out_specs=out_specs, check_vma=False
    )
```
